128 devices in a mesh: dp: 32 (over x, y, core), section: 4 (over z).
Axes of the slice: x: 4, y: 4, z: 4, core: 2. Of those that a mesh axis runs over, the one named last changes fastest.
Arguments:
- frames: bfloat16 [192, 512, 1280], P('dp'), may hold values from -6 to 6
- lengths: int32 [192], P('dp'), may hold values from 1 to 256, 24576 in all
- segments: int32 [192, 256], P('dp'), may hold values from 0 to 127, never falling along the last dimension, each value on 1 to 4 neighbouring positions
- section_weight: bfloat16 [4, 4096, 4096], P('section', 'dp'), may hold values from -0.09375 to 0.09375
- norm_gains: float32 [3, 4096], replicated, may hold values from 0.25 to 1.75
Outputs:
- section_out: bfloat16 [4, 192, 128, 4096], P('section', 'dp')
The draws below stay inside these ranges and needn't reach their ends.
All inputs are finite; a program needn't handle non-finite values. No bound on the sum of `lengths` on one device may be relied on, other than what follows from the above.
Results may differ from the reference program's by a relative error of at most 0.009.
Values may be sent and summed in bfloat16 or wider, within the bound.
No kernel may reach another device: no remote copies, remote signals or barrier semaphores. Data moves between devices by JAX's collectives and lax.ppermute only.
A program may use at most 192 MiB of HBM per device.

```python
import math
import jax
import jax.numpy as jnp
import numpy as np
from jax import lax

D = 4096
C = 1280
TAPS = 3
FIN = 512
N_SECTION_LAYERS = 3
FR2 = 256
TOKMB = 128
UTTS = 192
N_SECTION = 4


def block_levels(stream_key, extent, split, smallest, largest):
    def one(axis_at, blocks):
        heights = jax.random.uniform(jax.random.fold_in(jax.random.fold_in(stream_key, 6), axis_at), (blocks,), jnp.float32, smallest / len(split), largest / len(split))
        return jnp.repeat(jnp.exp(heights), extent[axis_at] // blocks).reshape((-1,) + (1,) * (len(extent) - axis_at - 1))

    level = one(*split[0])
    for cut in split[1:]:
        level = level * one(*cut)
    return level


def profile(number_of, total, bound, lean):
    weights = [(1 << 20) // math.isqrt(grade ** lean) + 1 for grade in range(2, number_of + 1)]
    rest, given = total - bound - (number_of - 1), [1] * (number_of - 1)
    while rest > 0:
        movable = [i for i in range(number_of - 1) if given[i] < bound]
        mass, remaining = sum([weights[i] for i in movable]), rest
        for i in movable:
            extra = min(bound - given[i], max(1, remaining * weights[i] // mass), rest)
            given[i] = given[i] + extra
            rest = rest - extra
    return np.array([bound] + given)


def uneven(rng, count, total, bound, slope):
    if count == 2:
        one = jax.random.randint(rng, (), max(1, total - bound), min(bound, total - 1) + 1)
        return jnp.stack([one, total - one])
    tallies = jnp.asarray(profile(count, total, bound, slope), jnp.int32)
    pairs = (count - 1) // 2
    source_of, receiver = tallies[1:1 + 2 * pairs:2], tallies[2:2 + 2 * pairs:2]
    slack = jnp.minimum(source_of - 1, bound - receiver)
    passed = jax.random.randint(jax.random.fold_in(rng, 1), (pairs,), 0, 1 << 20) % (slack + 1)
    tallies = tallies.at[1:1 + 2 * pairs:2].set(source_of - passed).at[2:2 + 2 * pairs:2].set(receiver + passed)
    return tallies[jax.random.permutation(jax.random.fold_in(rng, 2), count)]


def gaussian(own_key, shape, spread, most, cuts=(), kind=jnp.bfloat16):
    values = spread * jax.random.normal(own_key, shape, jnp.float32)
    if cuts:
        values = values * block_levels(own_key, shape, cuts, -0.22, 0.18)
    return jnp.clip(values, -most, most).astype(kind)


def setup_inputs(seed: int = 0) -> dict:
    streams_of = jax.random.split(jax.random.key(seed), 6)
    frames = gaussian(streams_of[0], (UTTS, FIN, C), 1.0, 6.0, ((0, 32),))
    lengths = uneven(streams_of[1], UTTS, UTTS * FR2 // 2, FR2, 2).astype(jnp.int32)
    segments = jax.vmap(lambda own: jnp.searchsorted(jnp.cumsum(uneven(own, TOKMB, FR2, 4, 1)), jnp.arange(FR2), side="right"))(jax.random.split(streams_of[2], UTTS)).reshape((UTTS, FR2)).astype(jnp.int32)
    section_weight = gaussian(streams_of[3], (N_SECTION, D, D), D ** -0.5, 0.09375, ((0, 4), (1, 32)))
    norm_gains = jnp.clip(1.0 + 0.15 * jax.random.normal(streams_of[4], (N_SECTION_LAYERS, D), jnp.float32), 0.25, 1.75)
    return {"frames": frames, "lengths": lengths, "segments": segments, "section_weight": section_weight, "norm_gains": norm_gains}


def encoder_part(frame_block, length, segment_row, kernel, projector, token_slots):
    half_frames = frame_block.shape[0] // 2
    channels = frame_block.shape[1]
    position = jnp.arange(frame_block.shape[0], dtype=jnp.int32)
    masked = jnp.where((position < 2 * length)[:, None], frame_block, jnp.zeros_like(frame_block))
    paired = masked.reshape(half_frames, 2 * channels)
    previous = jnp.concatenate([jnp.zeros((1, channels), masked.dtype), paired[:-1, channels:]], axis=0)
    stacked = jnp.concatenate([previous, paired], axis=1)
    hidden = jax.nn.gelu(jnp.dot(stacked, kernel, preferred_element_type=jnp.float32)).astype(jnp.bfloat16)
    frame_pos = jnp.arange(half_frames, dtype=jnp.int32)
    assigned = jnp.where(frame_pos < length, segment_row, -1)
    token_ids = jnp.arange(token_slots, dtype=jnp.int32)
    onehot = assigned[None, :] == token_ids[:, None]
    counts = lax.optimization_barrier(jnp.sum(onehot.astype(jnp.float32), axis=1))
    summed = jnp.dot(onehot.astype(jnp.bfloat16), hidden, preferred_element_type=jnp.float32)
    merged = (summed / jnp.maximum(counts, 1.0)[:, None]).astype(jnp.bfloat16)
    return jnp.dot(merged, projector, preferred_element_type=jnp.float32).astype(jnp.bfloat16)

def decoder_layer(token_rows, layer_gain, weight):
    values = token_rows.astype(jnp.float32)
    inverse_rms = lax.rsqrt(lax.optimization_barrier(jnp.mean(values * values, axis=-1, keepdims=True)) + 1e-06)
    normed = (values * inverse_rms * layer_gain).astype(jnp.bfloat16)
    return (values + jnp.dot(normed, weight, preferred_element_type=jnp.float32)).astype(jnp.bfloat16)

def reference(frames, lengths, segments, section_weight, norm_gains):
    flattened = section_weight[0].reshape(-1)
    kernel = flattened[:TAPS * C * C].reshape(TAPS * C, C)
    projector = flattened[TAPS * C * C:TAPS * C * C + C * D].reshape(C, D)

    def process(utterance):
        frame_block, length, segment_row = utterance
        current = encoder_part(frame_block, length, segment_row, kernel, projector, TOKMB)
        per_section = [current]
        for layer_index in range(N_SECTION - 1):
            current = decoder_layer(current, norm_gains[layer_index], section_weight[layer_index + 1])
            per_section.append(current)
        return jnp.stack(per_section)
    result = lax.map(process, (frames, lengths, segments))
    return jnp.transpose(result, (1, 0, 2, 3))
```

```python
import jax
import jax.numpy as jnp
from jax import lax
from jax.sharding import PartitionSpec as P


def encoder_part(frame_block, length, segment_row, kernel, projector, token_slots):
    half_frames = frame_block.shape[0] // 2
    channels = frame_block.shape[1]
    position = jnp.arange(frame_block.shape[0], dtype=jnp.int32)
    masked = jnp.where((position < 2 * length)[:, None], frame_block, jnp.zeros_like(frame_block))
    paired = masked.reshape(half_frames, 2 * channels)
    previous = jnp.concatenate(
        [jnp.zeros((1, channels), masked.dtype), paired[:-1, channels:]], axis=0
    )
    stacked = jnp.concatenate([previous, paired], axis=1)
    hidden = jax.nn.gelu(jnp.dot(stacked, kernel, preferred_element_type=jnp.float32)).astype(
        jnp.bfloat16
    )
    frame_pos = jnp.arange(half_frames, dtype=jnp.int32)
    assigned = jnp.where(frame_pos < length, segment_row, -1)
    token_ids = jnp.arange(token_slots, dtype=jnp.int32)
    onehot = assigned[None, :] == token_ids[:, None]
    counts = jnp.sum(onehot.astype(jnp.float32), axis=1)
    summed = jnp.dot(onehot.astype(jnp.bfloat16), hidden, preferred_element_type=jnp.float32)
    merged = (summed / jnp.maximum(counts, 1.0)[:, None]).astype(jnp.bfloat16)
    return jnp.dot(merged, projector, preferred_element_type=jnp.float32).astype(jnp.bfloat16)


def decoder_layer(token_rows, layer_gain, weight):
    values = token_rows.astype(jnp.float32)
    inverse_rms = lax.rsqrt(jnp.mean(values * values, axis=-1, keepdims=True) + 1e-06)
    normed = (values * inverse_rms * layer_gain).astype(jnp.bfloat16)
    return (values + jnp.dot(normed, weight, preferred_element_type=jnp.float32)).astype(
        jnp.bfloat16
    )


def per_device(frames, lengths, segments, section_weight, norm_gains):
    section_pos = lax.axis_index("section")
    sections = lax.axis_size("section")
    micro_count = frames.shape[0]
    tokens = frames.shape[1] // 4
    channels = frames.shape[2]
    model_width = section_weight.shape[2]

    section_slot = lax.all_gather(section_weight[0], "dp", axis=0, tiled=True)
    flattened = section_slot.reshape(-1)
    kernel = flattened[: 3 * channels * channels].reshape(3 * channels, channels)
    projector = flattened[
        3 * channels * channels : 3 * channels * channels + channels * model_width
    ].reshape(channels, model_width)
    layer_gain = norm_gains[jnp.maximum(section_pos - 1, 0)]

    lag = 2
    route = [(i, i + 1) for i in range(sections - 1)]
    ticks = micro_count + lag * (sections - 1)
    zeros = jnp.zeros((tokens, model_width), jnp.bfloat16)

    def tick_step(tick, state):
        pending, received, stored = state
        arrived = lax.ppermute(pending, "section", route)
        offset = tick - lag * section_pos
        active = (offset >= 0) & (offset < micro_count)
        micro_index = jnp.clip(offset, 0, micro_count - 1)

        def encode():
            return encoder_part(
                frames[micro_index],
                lengths[micro_index],
                segments[micro_index],
                kernel,
                projector,
                tokens,
            )

        def decode():
            return decoder_layer(received, layer_gain, section_slot)

        def work():
            return lax.cond(section_pos == 0, encode, decode)

        result = lax.cond(active, work, lambda: zeros)
        slot = jnp.where(active, micro_index, micro_count)
        stored = lax.dynamic_update_slice_in_dim(stored, result[None], slot, 0)
        return (result, arrived, stored)

    stored = jnp.zeros((micro_count + 1, tokens, model_width), jnp.bfloat16)
    _, _, stored = lax.fori_loop(0, ticks, tick_step, (zeros, zeros, stored))
    return stored[None, :micro_count]


def solution(mesh):
    return jax.shard_map(
        per_device,
        mesh=mesh,
        in_specs=(P("dp", None, None), P("dp"), P("dp", None), P("section", "dp", None), P()),
        out_specs=P("section", "dp", None, None),
        check_vma=False,
    )
```

```python
import jax
import jax.numpy as jnp
from jax import lax
from jax.sharding import PartitionSpec as P


def encoder_part(frame_block, length, segment_row, kernel, projector, token_slots):
    half_frames = frame_block.shape[0] // 2
    channels = frame_block.shape[1]
    position = jnp.arange(frame_block.shape[0], dtype=jnp.int32)
    masked = jnp.where((position < 2 * length)[:, None], frame_block, jnp.zeros_like(frame_block))
    paired = masked.reshape(half_frames, 2 * channels)
    previous = jnp.concatenate(
        [jnp.zeros((1, channels), masked.dtype), paired[:-1, channels:]], axis=0
    )
    stacked = jnp.concatenate([previous, paired], axis=1)
    hidden = jax.nn.gelu(jnp.dot(stacked, kernel, preferred_element_type=jnp.float32)).astype(
        jnp.bfloat16
    )
    frame_pos = jnp.arange(half_frames, dtype=jnp.int32)
    assigned = jnp.where(frame_pos < length, segment_row, -1)
    token_ids = jnp.arange(token_slots, dtype=jnp.int32)
    onehot = assigned[None, :] == token_ids[:, None]
    counts = jnp.sum(onehot.astype(jnp.float32), axis=1)
    summed = jnp.dot(onehot.astype(jnp.bfloat16), hidden, preferred_element_type=jnp.float32)
    merged = (summed / jnp.maximum(counts, 1.0)[:, None]).astype(jnp.bfloat16)
    return jnp.dot(merged, projector, preferred_element_type=jnp.float32).astype(jnp.bfloat16)


def decoder_layer(token_rows, layer_gain, weight):
    values = token_rows.astype(jnp.float32)
    inverse_rms = lax.rsqrt(jnp.mean(values * values, axis=-1, keepdims=True) + 1e-06)
    normed = (values * inverse_rms * layer_gain).astype(jnp.bfloat16)
    return (values + jnp.dot(normed, weight, preferred_element_type=jnp.float32)).astype(
        jnp.bfloat16
    )


def per_device(frames, lengths, segments, section_weight, norm_gains):
    section_pos = lax.axis_index("section")
    sections = lax.axis_size("section")
    micro_count = frames.shape[0]
    tokens = frames.shape[1] // 4
    channels = frames.shape[2]
    model_width = section_weight.shape[2]

    section_slot = lax.all_gather(section_weight[0], "dp", axis=0, tiled=True)
    kernel_rows = 3 * channels * channels // model_width
    projector_rows = channels
    kernel = section_slot[:kernel_rows].reshape(3 * channels, channels)
    projector = section_slot[kernel_rows : kernel_rows + projector_rows]
    layer_gain = norm_gains[jnp.maximum(section_pos - 1, 0)]

    lag = 2
    route = [(i, i + 1) for i in range(sections - 1)]
    ticks = micro_count + lag * (sections - 1)
    zeros = jnp.zeros((tokens, model_width), jnp.bfloat16)

    def tick_step(state, tick):
        pending, received = state
        arrived = lax.ppermute(pending, "section", route)
        offset = tick - lag * section_pos
        active = (offset >= 0) & (offset < micro_count)
        micro_index = jnp.clip(offset, 0, micro_count - 1)

        def encode():
            return encoder_part(
                frames[micro_index],
                lengths[micro_index],
                segments[micro_index],
                kernel,
                projector,
                tokens,
            )

        def decode():
            return decoder_layer(received, layer_gain, section_slot)

        def work():
            return lax.cond(section_pos == 0, encode, decode)

        result = lax.cond(active, work, lambda: zeros)
        return (result, arrived), result

    _, results = lax.scan(tick_step, (zeros, zeros), jnp.arange(ticks, dtype=jnp.int32))
    stored = lax.dynamic_slice_in_dim(results, lag * section_pos, micro_count, 0)
    return stored[None]


def solution(mesh):
    return jax.shard_map(
        per_device,
        mesh=mesh,
        in_specs=(P("dp", None, None), P("dp"), P("dp", None), P("section", "dp", None), P()),
        out_specs=P("section", "dp", None, None),
        check_vma=False,
    )
```

```python
import jax
import jax.numpy as jnp
from jax import lax
from jax.sharding import PartitionSpec as P


def encoder_part(frame_block, length, segment_row, kernel, projector, token_slots):
    half_frames = frame_block.shape[0] // 2
    channels = frame_block.shape[1]
    position = jnp.arange(frame_block.shape[0], dtype=jnp.int32)
    masked = jnp.where((position < 2 * length)[:, None], frame_block, jnp.zeros_like(frame_block))
    paired = masked.reshape(half_frames, 2 * channels)
    previous = jnp.concatenate(
        [jnp.zeros((1, channels), masked.dtype), paired[:-1, channels:]], axis=0
    )
    stacked = jnp.concatenate([previous, paired], axis=1)
    hidden = jax.nn.gelu(jnp.dot(stacked, kernel, preferred_element_type=jnp.float32)).astype(
        jnp.bfloat16
    )
    frame_pos = jnp.arange(half_frames, dtype=jnp.int32)
    assigned = jnp.where(frame_pos < length, segment_row, -1)
    token_ids = jnp.arange(token_slots, dtype=jnp.int32)
    onehot = assigned[None, :] == token_ids[:, None]
    counts = jnp.sum(onehot.astype(jnp.float32), axis=1)
    summed = jnp.dot(onehot.astype(jnp.bfloat16), hidden, preferred_element_type=jnp.float32)
    merged = (summed / jnp.maximum(counts, 1.0)[:, None]).astype(jnp.bfloat16)
    return jnp.dot(merged, projector, preferred_element_type=jnp.float32).astype(jnp.bfloat16)


def decoder_layer(token_rows, layer_gain, weight):
    values = token_rows.astype(jnp.float32)
    inverse_rms = lax.rsqrt(jnp.mean(values * values, axis=-1, keepdims=True) + 1e-06)
    normed = (values * inverse_rms * layer_gain).astype(jnp.bfloat16)
    return (values + jnp.dot(normed, weight, preferred_element_type=jnp.float32)).astype(
        jnp.bfloat16
    )


def per_device(frames, lengths, segments, section_weight, norm_gains):
    section_pos = lax.axis_index("section")
    sections = lax.axis_size("section")
    micro_count = frames.shape[0]
    tokens = frames.shape[1] // 4
    channels = frames.shape[2]
    model_width = section_weight.shape[2]

    across_chips = lax.all_gather(section_weight[0], "xy", axis=0, tiled=False)
    section_slot = lax.all_gather(across_chips, "core", axis=1, tiled=False).reshape(
        section_weight.shape[1] * lax.axis_size("xy") * lax.axis_size("core"), model_width
    )
    kernel_rows = 3 * channels * channels // model_width
    projector_rows = channels
    kernel = section_slot[:kernel_rows].reshape(3 * channels, channels)
    projector = section_slot[kernel_rows : kernel_rows + projector_rows]
    layer_gain = norm_gains[jnp.maximum(section_pos - 1, 0)]

    lag = 2
    route = [(i, i + 1) for i in range(sections - 1)]
    ticks = micro_count + lag * (sections - 1)
    zeros = jnp.zeros((tokens, model_width), jnp.bfloat16)

    def tick_step(state, tick):
        pending, received = state
        arrived = lax.ppermute(pending, "section", route)
        offset = tick - lag * section_pos
        active = (offset >= 0) & (offset < micro_count)
        micro_index = jnp.clip(offset, 0, micro_count - 1)

        def encode():
            return encoder_part(
                frames[micro_index],
                lengths[micro_index],
                segments[micro_index],
                kernel,
                projector,
                tokens,
            )

        def decode():
            return decoder_layer(received, layer_gain, section_slot)

        def work():
            return lax.cond(section_pos == 0, encode, decode)

        result = lax.cond(active, work, lambda: zeros)
        return (result, arrived), result

    _, results = lax.scan(tick_step, (zeros, zeros), jnp.arange(ticks, dtype=jnp.int32))
    stored = lax.dynamic_slice_in_dim(results, lag * section_pos, micro_count, 0)
    return stored[None]


def solution(mesh):
    cores = 2
    devices = mesh.devices.reshape(mesh.shape["dp"] // cores, cores, mesh.shape["section"])
    split_mesh = jax.sharding.Mesh(devices, ("xy", "core", "section"))
    dp = ("xy", "core")
    return jax.shard_map(
        per_device,
        mesh=split_mesh,
        in_specs=(P(dp, None, None), P(dp), P(dp, None), P("section", dp, None), P()),
        out_specs=P("section", dp, None, None),
        check_vma=False,
    )
```

```python
import jax
import jax.numpy as jnp
from jax import lax
from jax.sharding import PartitionSpec as P


def encoder_part(frame_block, length, segment_row, kernel, projector, token_slots):
    half_frames = frame_block.shape[0] // 2
    channels = frame_block.shape[1]
    position = jnp.arange(frame_block.shape[0], dtype=jnp.int32)
    masked = jnp.where((position < 2 * length)[:, None], frame_block, jnp.zeros_like(frame_block))
    paired = masked.reshape(half_frames, 2 * channels)
    previous = jnp.concatenate(
        [jnp.zeros((1, channels), masked.dtype), paired[:-1, channels:]], axis=0
    )
    stacked = jnp.concatenate([previous, paired], axis=1)
    hidden = jax.nn.gelu(jnp.dot(stacked, kernel, preferred_element_type=jnp.float32)).astype(
        jnp.bfloat16
    )
    frame_pos = jnp.arange(half_frames, dtype=jnp.int32)
    assigned = jnp.where(frame_pos < length, segment_row, -1)
    token_ids = jnp.arange(token_slots, dtype=jnp.int32)
    onehot = assigned[None, :] == token_ids[:, None]
    counts = jnp.sum(onehot.astype(jnp.float32), axis=1)
    summed = jnp.dot(onehot.astype(jnp.bfloat16), hidden, preferred_element_type=jnp.float32)
    merged = (summed / jnp.maximum(counts, 1.0)[:, None]).astype(jnp.bfloat16)
    return jnp.dot(merged, projector, preferred_element_type=jnp.float32).astype(jnp.bfloat16)


def decoder_layer(token_rows, layer_gain, weight):
    values = token_rows.astype(jnp.float32)
    inverse_rms = lax.rsqrt(jnp.mean(values * values, axis=-1, keepdims=True) + 1e-06)
    normed = (values * inverse_rms * layer_gain).astype(jnp.bfloat16)
    return (values + jnp.dot(normed, weight, preferred_element_type=jnp.float32)).astype(
        jnp.bfloat16
    )


def per_device(frames, lengths, segments, section_weight, norm_gains):
    section_pos = lax.axis_index("section")
    sections = lax.axis_size("section")
    micro_count = frames.shape[0]
    tokens = frames.shape[1] // 4
    channels = frames.shape[2]
    model_width = section_weight.shape[2]

    section_slot = lax.all_gather(section_weight[0], "dp", axis=0, tiled=True)
    flattened = section_slot.reshape(-1)
    kernel = flattened[: 3 * channels * channels].reshape(3 * channels, channels)
    projector = flattened[
        3 * channels * channels : 3 * channels * channels + channels * model_width
    ].reshape(channels, model_width)
    layer_gain = norm_gains[jnp.maximum(section_pos - 1, 0)]

    lag = 2
    route = [(i, i + 1) for i in range(sections - 1)]
    ticks = micro_count + lag * (sections - 1)
    zeros = jnp.zeros((tokens, model_width), jnp.bfloat16)

    def tick_step(tick, state):
        pending, received, stored = state
        arrived = lax.ppermute(pending, "section", route)
        offset = tick - lag * section_pos
        active = (offset >= 0) & (offset < micro_count)
        micro_index = jnp.clip(offset, 0, micro_count - 1)

        def encode():
            return encoder_part(
                frames[micro_index],
                lengths[micro_index],
                segments[micro_index],
                kernel,
                projector,
                tokens,
            )

        def decode():
            return decoder_layer(received, layer_gain, section_slot)

        def work():
            return lax.cond(section_pos == 0, encode, decode)

        result = lax.cond(active, work, lambda: zeros)
        slot = jnp.where(active, micro_index, micro_count)
        stored = lax.dynamic_update_slice_in_dim(stored, result, slot * tokens, 0)
        return (result, arrived, stored)

    stored = jnp.zeros(((micro_count + 1) * tokens, model_width), jnp.bfloat16)
    _, _, stored = lax.fori_loop(0, ticks, tick_step, (zeros, zeros, stored))
    return stored[: micro_count * tokens].reshape(1, micro_count, tokens, model_width)


def solution(mesh):
    return jax.shard_map(
        per_device,
        mesh=mesh,
        in_specs=(P("dp", None, None), P("dp"), P("dp", None), P("section", "dp", None), P()),
        out_specs=P("section", "dp", None, None),
        check_vma=False,
    )
```

```python
import jax
import jax.numpy as jnp
from jax import lax
from jax.sharding import PartitionSpec as P


def encoder_part(frame_block, length, segment_row, kernel, projector, token_slots):
    half_frames = frame_block.shape[0] // 2
    channels = frame_block.shape[1]
    position = jnp.arange(frame_block.shape[0], dtype=jnp.int32)
    masked = jnp.where((position < 2 * length)[:, None], frame_block, jnp.zeros_like(frame_block))
    paired = masked.reshape(half_frames, 2 * channels)
    previous = jnp.concatenate(
        [jnp.zeros((1, channels), masked.dtype), paired[:-1, channels:]], axis=0
    )
    stacked = jnp.concatenate([previous, paired], axis=1)
    hidden = jax.nn.gelu(jnp.dot(stacked, kernel, preferred_element_type=jnp.float32)).astype(
        jnp.bfloat16
    )
    frame_pos = jnp.arange(half_frames, dtype=jnp.int32)
    assigned = jnp.where(frame_pos < length, segment_row, -1)
    token_ids = jnp.arange(token_slots, dtype=jnp.int32)
    onehot = assigned[None, :] == token_ids[:, None]
    counts = jnp.sum(onehot.astype(jnp.float32), axis=1)
    summed = jnp.dot(onehot.astype(jnp.bfloat16), hidden, preferred_element_type=jnp.float32)
    merged = (summed / jnp.maximum(counts, 1.0)[:, None]).astype(jnp.bfloat16)
    return jnp.dot(merged, projector, preferred_element_type=jnp.float32).astype(jnp.bfloat16)


def decoder_layer(token_rows, layer_gain, weight):
    values = token_rows.astype(jnp.float32)
    inverse_rms = lax.rsqrt(jnp.mean(values * values, axis=-1, keepdims=True) + 1e-06)
    normed = (values * inverse_rms * layer_gain).astype(jnp.bfloat16)
    return (values + jnp.dot(normed, weight, preferred_element_type=jnp.float32)).astype(
        jnp.bfloat16
    )


def per_device(frames, lengths, segments, section_weight, norm_gains):
    section_pos = lax.axis_index("section")
    sections = lax.axis_size("section")
    micro_count = frames.shape[0]
    tokens = frames.shape[1] // 4
    channels = frames.shape[2]
    model_width = section_weight.shape[2]

    section_slot = lax.all_gather(section_weight[0], "dp", axis=0, tiled=True)
    flattened = section_slot.reshape(-1)
    kernel = flattened[: 3 * channels * channels].reshape(3 * channels, channels)
    projector = flattened[
        3 * channels * channels : 3 * channels * channels + channels * model_width
    ].reshape(channels, model_width)
    layer_gain = norm_gains[jnp.maximum(section_pos - 1, 0)]

    lag = 2
    route = [(i, i + 1) for i in range(sections - 1)]
    ticks = micro_count + lag * (sections - 1)
    zeros = jnp.zeros((tokens, model_width), jnp.bfloat16)

    def one_tick(tick, pending, received, stored):
        arrived = lax.ppermute(pending, "section", route)
        offset = tick - lag * section_pos
        active = (offset >= 0) & (offset < micro_count)
        micro_index = jnp.clip(offset, 0, micro_count - 1)

        def encode():
            return encoder_part(
                frames[micro_index],
                lengths[micro_index],
                segments[micro_index],
                kernel,
                projector,
                tokens,
            )

        def decode():
            return decoder_layer(received, layer_gain, section_slot)

        def work():
            return lax.cond(section_pos == 0, encode, decode)

        result = lax.cond(active, work, lambda: zeros)
        slot = jnp.where(active, micro_index, micro_count)
        stored = lax.dynamic_update_slice_in_dim(stored, result, slot * tokens, 0)
        return result, arrived, stored

    def tick_pair(pair, state):
        pending, received, stored = state
        pending, received, stored = one_tick(2 * pair, pending, received, stored)
        return one_tick(2 * pair + 1, pending, received, stored)

    stored = jnp.zeros(((micro_count + 1) * tokens, model_width), jnp.bfloat16)
    _, _, stored = lax.fori_loop(0, ticks // 2, tick_pair, (zeros, zeros, stored))
    return stored[: micro_count * tokens].reshape(1, micro_count, tokens, model_width)


def solution(mesh):
    return jax.shard_map(
        per_device,
        mesh=mesh,
        in_specs=(P("dp", None, None), P("dp"), P("dp", None), P("section", "dp", None), P()),
        out_specs=P("section", "dp", None, None),
        check_vma=False,
    )
```

```python
import jax
import jax.numpy as jnp
from jax import lax
from jax.sharding import PartitionSpec as P


def encoder_part(frame_block, length, segment_row, kernel, projector, token_slots):
    half_frames = frame_block.shape[0] // 2
    channels = frame_block.shape[1]
    position = jnp.arange(frame_block.shape[0], dtype=jnp.int32)
    masked = jnp.where((position < 2 * length)[:, None], frame_block, jnp.zeros_like(frame_block))
    paired = masked.reshape(half_frames, 2 * channels)
    previous = jnp.concatenate(
        [jnp.zeros((1, channels), masked.dtype), paired[:-1, channels:]], axis=0
    )
    stacked = jnp.concatenate([previous, paired], axis=1)
    hidden = jax.nn.gelu(jnp.dot(stacked, kernel, preferred_element_type=jnp.float32)).astype(
        jnp.bfloat16
    )
    frame_pos = jnp.arange(half_frames, dtype=jnp.int32)
    assigned = jnp.where(frame_pos < length, segment_row, -1)
    token_ids = jnp.arange(token_slots, dtype=jnp.int32)
    onehot = assigned[None, :] == token_ids[:, None]
    counts = jnp.sum(onehot.astype(jnp.float32), axis=1)
    summed = jnp.dot(onehot.astype(jnp.bfloat16), hidden, preferred_element_type=jnp.float32)
    merged = (summed / jnp.maximum(counts, 1.0)[:, None]).astype(jnp.bfloat16)
    return jnp.dot(merged, projector, preferred_element_type=jnp.float32).astype(jnp.bfloat16)


def decoder_layer(token_rows, layer_gain, weight):
    values = token_rows.astype(jnp.float32)
    inverse_rms = lax.rsqrt(jnp.mean(values * values, axis=-1, keepdims=True) + 1e-06)
    normed = (values * inverse_rms * layer_gain).astype(jnp.bfloat16)
    return (values + jnp.dot(normed, weight, preferred_element_type=jnp.float32)).astype(
        jnp.bfloat16
    )


def per_device(frames, lengths, segments, section_weight, norm_gains):
    section_pos = lax.axis_index("section")
    sections = lax.axis_size("section")
    micro_count = frames.shape[0]
    tokens = frames.shape[1] // 4
    channels = frames.shape[2]
    model_width = section_weight.shape[2]

    section_slot = lax.all_gather(section_weight[0], "dp", axis=0, tiled=True)
    flattened = section_slot.reshape(-1)
    kernel = flattened[: 3 * channels * channels].reshape(3 * channels, channels)
    projector = flattened[
        3 * channels * channels : 3 * channels * channels + channels * model_width
    ].reshape(channels, model_width)
    layer_gain = norm_gains[jnp.maximum(section_pos - 1, 0)]

    lag = 2
    route = [(i, i + 1) for i in range(sections - 1)]
    ticks = micro_count + lag * (sections - 1)
    zeros = jnp.zeros((tokens, model_width), jnp.bfloat16)

    def one_tick(tick, pending, received, stored):
        arrived = lax.ppermute(pending, "section", route)
        offset = tick - lag * section_pos
        active = (offset >= 0) & (offset < micro_count)
        micro_index = jnp.clip(offset, 0, micro_count - 1)

        def encode():
            return encoder_part(
                frames[micro_index],
                lengths[micro_index],
                segments[micro_index],
                kernel,
                projector,
                tokens,
            )

        def decode():
            return decoder_layer(received, layer_gain, section_slot)

        def work():
            return lax.cond(section_pos == 0, encode, decode)

        def keep():
            return lax.dynamic_slice_in_dim(stored, micro_index * tokens, tokens, 0)

        result = lax.cond(active, work, keep)
        stored = lax.dynamic_update_slice_in_dim(stored, result, micro_index * tokens, 0)
        return result, arrived, stored

    def tick_pair(pair, state):
        pending, received, stored = state
        pending, received, stored = one_tick(2 * pair, pending, received, stored)
        return one_tick(2 * pair + 1, pending, received, stored)

    stored = jnp.zeros((micro_count * tokens, model_width), jnp.bfloat16)
    _, _, stored = lax.fori_loop(0, ticks // 2, tick_pair, (zeros, zeros, stored))
    return stored.reshape(1, micro_count, tokens, model_width)


def solution(mesh):
    return jax.shard_map(
        per_device,
        mesh=mesh,
        in_specs=(P("dp", None, None), P("dp"), P("dp", None), P("section", "dp", None), P()),
        out_specs=P("section", "dp", None, None),
        check_vma=False,
    )
```

```python
import jax
import jax.numpy as jnp
from jax import lax
from jax.experimental import pallas as pl
from jax.sharding import PartitionSpec as P


def rows_matmul(left, weight, first_row, residual=None, column_block=512):
    rows, depth = left.shape
    width = weight.shape[1]

    def kernel(left_ref, weight_ref, *rest):
        out_ref = rest[-1]
        acc = jnp.dot(left_ref[...], weight_ref[...], preferred_element_type=jnp.float32)
        if residual is not None:
            acc = acc + rest[0][...].astype(jnp.float32)
        out_ref[...] = acc.astype(out_ref.dtype)

    in_specs = [
        pl.BlockSpec((rows, depth), lambda n: (0, 0)),
        pl.BlockSpec(
            (pl.Element(depth), pl.Element(column_block)),
            lambda n: (first_row, n * column_block),
        ),
    ]
    operands = [left, weight]
    if residual is not None:
        in_specs.append(pl.BlockSpec((rows, column_block), lambda n: (0, n)))
        operands.append(residual)
    return pl.pallas_call(
        kernel,
        grid=(width // column_block,),
        in_specs=in_specs,
        out_specs=pl.BlockSpec((rows, column_block), lambda n: (0, n)),
        out_shape=jax.ShapeDtypeStruct((rows, width), jnp.bfloat16),
    )(*operands)


def encoder_part(frame_block, length, segment_row, kernel, slot, projector_row, token_slots):
    half_frames = frame_block.shape[0] // 2
    channels = frame_block.shape[1]
    position = jnp.arange(frame_block.shape[0], dtype=jnp.int32)
    masked = jnp.where((position < 2 * length)[:, None], frame_block, jnp.zeros_like(frame_block))
    paired = masked.reshape(half_frames, 2 * channels)
    previous = jnp.concatenate(
        [jnp.zeros((1, channels), masked.dtype), paired[:-1, channels:]], axis=0
    )
    stacked = jnp.concatenate([previous, paired], axis=1)
    hidden = jax.nn.gelu(jnp.dot(stacked, kernel, preferred_element_type=jnp.float32)).astype(
        jnp.bfloat16
    )
    frame_pos = jnp.arange(half_frames, dtype=jnp.int32)
    assigned = jnp.where(frame_pos < length, segment_row, -1)
    token_ids = jnp.arange(token_slots, dtype=jnp.int32)
    onehot = assigned[None, :] == token_ids[:, None]
    counts = jnp.sum(onehot.astype(jnp.float32), axis=1)
    summed = jnp.dot(onehot.astype(jnp.bfloat16), hidden, preferred_element_type=jnp.float32)
    merged = (summed / jnp.maximum(counts, 1.0)[:, None]).astype(jnp.bfloat16)
    return rows_matmul(merged, slot, projector_row)


def decoder_layer(token_rows, layer_gain, weight):
    values = token_rows.astype(jnp.float32)
    inverse_rms = lax.rsqrt(jnp.mean(values * values, axis=-1, keepdims=True) + 1e-06)
    normed = (values * inverse_rms * layer_gain).astype(jnp.bfloat16)
    return rows_matmul(normed, weight, 0, residual=token_rows)


def per_device(frames, lengths, segments, section_weight, norm_gains):
    section_pos = lax.axis_index("section")
    sections = lax.axis_size("section")
    micro_count = frames.shape[0]
    tokens = frames.shape[1] // 4
    channels = frames.shape[2]
    model_width = section_weight.shape[2]

    section_slot = lax.all_gather(section_weight[0], "dp", axis=0, tiled=True)
    kernel_rows = 3 * channels * channels // model_width
    kernel = section_slot[:kernel_rows].reshape(3 * channels, channels)
    layer_gain = norm_gains[jnp.maximum(section_pos - 1, 0)]

    lag = 2
    route = [(i, i + 1) for i in range(sections - 1)]
    ticks = micro_count + lag * (sections - 1)
    zeros = jnp.zeros((tokens, model_width), jnp.bfloat16)

    def one_tick(tick, pending, received, stored):
        arrived = lax.ppermute(pending, "section", route)
        offset = tick - lag * section_pos
        active = (offset >= 0) & (offset < micro_count)
        micro_index = jnp.clip(offset, 0, micro_count - 1)

        def encode():
            return encoder_part(
                frames[micro_index],
                lengths[micro_index],
                segments[micro_index],
                kernel,
                section_slot,
                kernel_rows,
                tokens,
            )

        def decode():
            return decoder_layer(received, layer_gain, section_slot)

        def work():
            return lax.cond(section_pos == 0, encode, decode)

        def keep():
            return lax.dynamic_slice_in_dim(stored, micro_index * tokens, tokens, 0)

        result = lax.cond(active, work, keep)
        stored = lax.dynamic_update_slice_in_dim(stored, result, micro_index * tokens, 0)
        return result, arrived, stored

    def tick_pair(pair, state):
        pending, received, stored = state
        pending, received, stored = one_tick(2 * pair, pending, received, stored)
        return one_tick(2 * pair + 1, pending, received, stored)

    stored = jnp.zeros((micro_count * tokens, model_width), jnp.bfloat16)
    _, _, stored = lax.fori_loop(0, ticks // 2, tick_pair, (zeros, zeros, stored))
    return stored.reshape(1, micro_count, tokens, model_width)


def solution(mesh):
    return jax.shard_map(
        per_device,
        mesh=mesh,
        in_specs=(P("dp", None, None), P("dp"), P("dp", None), P("section", "dp", None), P()),
        out_specs=P("section", "dp", None, None),
        check_vma=False,
    )
```

```python
import jax
import jax.numpy as jnp
from jax import lax
from jax.experimental import pallas as pl
from jax.sharding import PartitionSpec as P


def rows_matmul(left, weight, first_row, residual=None, column_block=512):
    rows, depth = left.shape
    width = weight.shape[1]

    def kernel(left_ref, weight_ref, *rest):
        out_ref = rest[-1]
        acc = jnp.dot(left_ref[...], weight_ref[...], preferred_element_type=jnp.float32)
        if residual is not None:
            acc = acc + rest[0][...].astype(jnp.float32)
        out_ref[...] = acc.astype(out_ref.dtype)

    in_specs = [
        pl.BlockSpec((rows, depth), lambda n: (0, 0)),
        pl.BlockSpec(
            (pl.Element(depth), pl.Element(column_block)),
            lambda n: (first_row, n * column_block),
        ),
    ]
    operands = [left, weight]
    if residual is not None:
        in_specs.append(pl.BlockSpec((rows, column_block), lambda n: (0, n)))
        operands.append(residual)
    return pl.pallas_call(
        kernel,
        grid=(width // column_block,),
        in_specs=in_specs,
        out_specs=pl.BlockSpec((rows, column_block), lambda n: (0, n)),
        out_shape=jax.ShapeDtypeStruct((rows, width), jnp.bfloat16),
    )(*operands)


def encoder_part(frame_block, length, segment_row, kernel, projector, token_slots):
    half_frames = frame_block.shape[0] // 2
    channels = frame_block.shape[1]
    position = jnp.arange(frame_block.shape[0], dtype=jnp.int32)
    masked = jnp.where((position < 2 * length)[:, None], frame_block, jnp.zeros_like(frame_block))
    paired = masked.reshape(half_frames, 2 * channels)
    previous = jnp.concatenate(
        [jnp.zeros((1, channels), masked.dtype), paired[:-1, channels:]], axis=0
    )
    stacked = jnp.concatenate([previous, paired], axis=1)
    hidden = jax.nn.gelu(jnp.dot(stacked, kernel, preferred_element_type=jnp.float32)).astype(
        jnp.bfloat16
    )
    frame_pos = jnp.arange(half_frames, dtype=jnp.int32)
    assigned = jnp.where(frame_pos < length, segment_row, -1)
    token_ids = jnp.arange(token_slots, dtype=jnp.int32)
    onehot = assigned[None, :] == token_ids[:, None]
    counts = jnp.sum(onehot.astype(jnp.float32), axis=1)
    summed = jnp.dot(onehot.astype(jnp.bfloat16), hidden, preferred_element_type=jnp.float32)
    merged = (summed / jnp.maximum(counts, 1.0)[:, None]).astype(jnp.bfloat16)
    return jnp.dot(merged, projector, preferred_element_type=jnp.float32).astype(jnp.bfloat16)


def decoder_layer(token_rows, layer_gain, weight):
    values = token_rows.astype(jnp.float32)
    inverse_rms = lax.rsqrt(jnp.mean(values * values, axis=-1, keepdims=True) + 1e-06)
    normed = (values * inverse_rms * layer_gain).astype(jnp.bfloat16)
    return rows_matmul(normed, weight, 0, residual=token_rows)


def per_device(frames, lengths, segments, section_weight, norm_gains):
    section_pos = lax.axis_index("section")
    sections = lax.axis_size("section")
    micro_count = frames.shape[0]
    tokens = frames.shape[1] // 4
    channels = frames.shape[2]
    model_width = section_weight.shape[2]

    section_slot = lax.all_gather(section_weight[0], "dp", axis=0, tiled=True)
    kernel_rows = 3 * channels * channels // model_width
    kernel = section_slot[:kernel_rows].reshape(3 * channels, channels)
    projector = section_slot[kernel_rows : kernel_rows + channels]
    layer_gain = norm_gains[jnp.maximum(section_pos - 1, 0)]

    lag = 2
    route = [(i, i + 1) for i in range(sections - 1)]
    ticks = micro_count + lag * (sections - 1)
    zeros = jnp.zeros((tokens, model_width), jnp.bfloat16)

    def one_tick(tick, pending, received, stored):
        arrived = lax.ppermute(pending, "section", route)
        offset = tick - lag * section_pos
        active = (offset >= 0) & (offset < micro_count)
        micro_index = jnp.clip(offset, 0, micro_count - 1)

        def encode():
            return encoder_part(
                frames[micro_index],
                lengths[micro_index],
                segments[micro_index],
                kernel,
                projector,
                tokens,
            )

        def decode():
            return decoder_layer(received, layer_gain, section_slot)

        def work():
            return lax.cond(section_pos == 0, encode, decode)

        def keep():
            return lax.dynamic_slice_in_dim(stored, micro_index * tokens, tokens, 0)

        result = lax.cond(active, work, keep)
        stored = lax.dynamic_update_slice_in_dim(stored, result, micro_index * tokens, 0)
        return result, arrived, stored

    def tick_pair(pair, state):
        pending, received, stored = state
        pending, received, stored = one_tick(2 * pair, pending, received, stored)
        return one_tick(2 * pair + 1, pending, received, stored)

    stored = jnp.zeros((micro_count * tokens, model_width), jnp.bfloat16)
    _, _, stored = lax.fori_loop(0, ticks // 2, tick_pair, (zeros, zeros, stored))
    return stored.reshape(1, micro_count, tokens, model_width)


def solution(mesh):
    return jax.shard_map(
        per_device,
        mesh=mesh,
        in_specs=(P("dp", None, None), P("dp"), P("dp", None), P("section", "dp", None), P()),
        out_specs=P("section", "dp", None, None),
        check_vma=False,
    )
```

```python
import jax
import jax.numpy as jnp
from jax import lax
from jax.sharding import PartitionSpec as P


def encoder_inputs(frame_block, length, segment_row, token_slots):
    half_frames = frame_block.shape[0] // 2
    channels = frame_block.shape[1]
    position = jnp.arange(frame_block.shape[0], dtype=jnp.int32)
    masked = jnp.where((position < 2 * length)[:, None], frame_block, jnp.zeros_like(frame_block))
    paired = masked.reshape(half_frames, 2 * channels)
    previous = jnp.concatenate(
        [jnp.zeros((1, channels), masked.dtype), paired[:-1, channels:]], axis=0
    )
    stacked = jnp.concatenate([previous, paired], axis=1)
    frame_pos = jnp.arange(half_frames, dtype=jnp.int32)
    assigned = jnp.where(frame_pos < length, segment_row, -1)
    token_ids = jnp.arange(token_slots, dtype=jnp.int32)
    onehot = assigned[None, :] == token_ids[:, None]
    counts = jnp.sum(onehot.astype(jnp.float32), axis=1)
    return stacked, onehot.astype(jnp.bfloat16), jnp.maximum(counts, 1.0)


def encoder_part(stacked, onehot, counts, kernel, projector):
    hidden = jax.nn.gelu(jnp.dot(stacked, kernel, preferred_element_type=jnp.float32)).astype(
        jnp.bfloat16
    )
    summed = jnp.dot(onehot, hidden, preferred_element_type=jnp.float32)
    merged = (summed / counts[:, None]).astype(jnp.bfloat16)
    return jnp.dot(merged, projector, preferred_element_type=jnp.float32).astype(jnp.bfloat16)


def decoder_layer(token_rows, layer_gain, weight):
    values = token_rows.astype(jnp.float32)
    inverse_rms = lax.rsqrt(jnp.mean(values * values, axis=-1, keepdims=True) + 1e-06)
    normed = (values * inverse_rms * layer_gain).astype(jnp.bfloat16)
    return (values + jnp.dot(normed, weight, preferred_element_type=jnp.float32)).astype(
        jnp.bfloat16
    )


def per_device(frames, lengths, segments, section_weight, norm_gains):
    section_pos = lax.axis_index("section")
    sections = lax.axis_size("section")
    micro_count = frames.shape[0]
    tokens = frames.shape[1] // 4
    channels = frames.shape[2]
    model_width = section_weight.shape[2]

    section_slot = lax.all_gather(section_weight[0], "dp", axis=0, tiled=True)
    flattened = section_slot.reshape(-1)
    kernel = flattened[: 3 * channels * channels].reshape(3 * channels, channels)
    projector = flattened[
        3 * channels * channels : 3 * channels * channels + channels * model_width
    ].reshape(channels, model_width)
    layer_gain = norm_gains[jnp.maximum(section_pos - 1, 0)]
    stacked_all, onehot_all, counts_all = jax.vmap(
        lambda f, n, s: encoder_inputs(f, n, s, tokens)
    )(frames, lengths, segments)

    lag = 2
    route = [(i, i + 1) for i in range(sections - 1)]
    ticks = micro_count + lag * (sections - 1)
    zeros = jnp.zeros((tokens, model_width), jnp.bfloat16)

    def one_tick(tick, pending, received, stored):
        arrived = lax.ppermute(pending, "section", route)
        offset = tick - lag * section_pos
        active = (offset >= 0) & (offset < micro_count)
        micro_index = jnp.clip(offset, 0, micro_count - 1)

        def encode():
            return encoder_part(
                stacked_all[micro_index],
                onehot_all[micro_index],
                counts_all[micro_index],
                kernel,
                projector,
            )

        def decode():
            return decoder_layer(received, layer_gain, section_slot)

        def work():
            return lax.cond(section_pos == 0, encode, decode)

        def keep():
            return lax.dynamic_slice_in_dim(stored, micro_index * tokens, tokens, 0)

        result = lax.cond(active, work, keep)
        stored = lax.dynamic_update_slice_in_dim(stored, result, micro_index * tokens, 0)
        return result, arrived, stored

    def tick_pair(pair, state):
        pending, received, stored = state
        pending, received, stored = one_tick(2 * pair, pending, received, stored)
        return one_tick(2 * pair + 1, pending, received, stored)

    stored = jnp.zeros((micro_count * tokens, model_width), jnp.bfloat16)
    _, _, stored = lax.fori_loop(0, ticks // 2, tick_pair, (zeros, zeros, stored))
    return stored.reshape(1, micro_count, tokens, model_width)


def solution(mesh):
    return jax.shard_map(
        per_device,
        mesh=mesh,
        in_specs=(P("dp", None, None), P("dp"), P("dp", None), P("section", "dp", None), P()),
        out_specs=P("section", "dp", None, None),
        check_vma=False,
    )
```

```python
import jax
import jax.numpy as jnp
from jax import lax
from jax.sharding import PartitionSpec as P


def encoder_inputs(frame_block, length, segment_row, token_slots):
    half_frames = frame_block.shape[0] // 2
    channels = frame_block.shape[1]
    position = jnp.arange(frame_block.shape[0], dtype=jnp.int32)
    masked = jnp.where((position < 2 * length)[:, None], frame_block, jnp.zeros_like(frame_block))
    paired = masked.reshape(half_frames, 2 * channels)
    previous = jnp.concatenate(
        [jnp.zeros((1, channels), masked.dtype), paired[:-1, channels:]], axis=0
    )
    stacked = jnp.concatenate([previous, paired], axis=1)
    frame_pos = jnp.arange(half_frames, dtype=jnp.int32)
    assigned = jnp.where(frame_pos < length, segment_row, -1)
    token_ids = jnp.arange(token_slots, dtype=jnp.int32)
    onehot = assigned[None, :] == token_ids[:, None]
    counts = jnp.sum(onehot.astype(jnp.float32), axis=1)
    return stacked, onehot.astype(jnp.bfloat16), jnp.maximum(counts, 1.0)


def encoder_part(stacked, onehot, counts, kernel, projector):
    hidden = jax.nn.gelu(jnp.dot(stacked, kernel, preferred_element_type=jnp.float32)).astype(
        jnp.bfloat16
    )
    summed = jnp.dot(onehot, hidden, preferred_element_type=jnp.float32)
    merged = (summed / counts[:, None]).astype(jnp.bfloat16)
    return jnp.dot(merged, projector, preferred_element_type=jnp.float32).astype(jnp.bfloat16)


def decoder_layer(token_rows, layer_gain, weight):
    values = token_rows.astype(jnp.float32)
    inverse_rms = lax.rsqrt(jnp.mean(values * values, axis=-1, keepdims=True) + 1e-06)
    normed = (values * inverse_rms * layer_gain).astype(jnp.bfloat16)
    return (values + jnp.dot(normed, weight, preferred_element_type=jnp.float32)).astype(
        jnp.bfloat16
    )


def per_device(frames, lengths, segments, section_weight, norm_gains):
    section_pos = lax.axis_index("section")
    sections = lax.axis_size("section")
    micro_count = frames.shape[0]
    tokens = frames.shape[1] // 4
    channels = frames.shape[2]
    model_width = section_weight.shape[2]

    section_slot = lax.all_gather(section_weight[0], "dp", axis=0, tiled=True)
    tap_rows = channels * channels // model_width
    kernel = jnp.concatenate(
        [
            section_slot[k * tap_rows : (k + 1) * tap_rows].reshape(channels, channels)
            for k in range(3)
        ],
        axis=0,
    )
    projector = section_slot[3 * tap_rows : 3 * tap_rows + channels]
    layer_gain = norm_gains[jnp.maximum(section_pos - 1, 0)]
    stacked_all, onehot_all, counts_all = jax.vmap(
        lambda f, n, s: encoder_inputs(f, n, s, tokens)
    )(frames, lengths, segments)

    lag = 2
    route = [(i, i + 1) for i in range(sections - 1)]
    ticks = micro_count + lag * (sections - 1)
    zeros = jnp.zeros((tokens, model_width), jnp.bfloat16)

    def one_tick(tick, pending, received, stored):
        arrived = lax.ppermute(pending, "section", route)
        offset = tick - lag * section_pos
        active = (offset >= 0) & (offset < micro_count)
        micro_index = jnp.clip(offset, 0, micro_count - 1)

        def encode():
            return encoder_part(
                stacked_all[micro_index],
                onehot_all[micro_index],
                counts_all[micro_index],
                kernel,
                projector,
            )

        def decode():
            return decoder_layer(received, layer_gain, section_slot)

        def work():
            return lax.cond(section_pos == 0, encode, decode)

        def keep():
            return lax.dynamic_slice_in_dim(stored, micro_index * tokens, tokens, 0)

        result = lax.cond(active, work, keep)
        stored = lax.dynamic_update_slice_in_dim(stored, result, micro_index * tokens, 0)
        return result, arrived, stored

    def tick_pair(pair, state):
        pending, received, stored = state
        pending, received, stored = one_tick(2 * pair, pending, received, stored)
        return one_tick(2 * pair + 1, pending, received, stored)

    stored = jnp.zeros((micro_count * tokens, model_width), jnp.bfloat16)
    _, _, stored = lax.fori_loop(0, ticks // 2, tick_pair, (zeros, zeros, stored))
    return stored.reshape(1, micro_count, tokens, model_width)


def solution(mesh):
    return jax.shard_map(
        per_device,
        mesh=mesh,
        in_specs=(P("dp", None, None), P("dp"), P("dp", None), P("section", "dp", None), P()),
        out_specs=P("section", "dp", None, None),
        check_vma=False,
    )
```

```python
import jax
import jax.numpy as jnp
from jax import lax
from jax.sharding import PartitionSpec as P


def encoder_inputs(frame_block, length, segment_row, token_slots):
    half_frames = frame_block.shape[0] // 2
    channels = frame_block.shape[1]
    position = jnp.arange(frame_block.shape[0], dtype=jnp.int32)
    masked = jnp.where((position < 2 * length)[:, None], frame_block, jnp.zeros_like(frame_block))
    paired = masked.reshape(half_frames, 2 * channels)
    previous = jnp.concatenate(
        [jnp.zeros((1, channels), masked.dtype), paired[:-1, channels:]], axis=0
    )
    stacked = jnp.concatenate([previous, paired], axis=1)
    frame_pos = jnp.arange(half_frames, dtype=jnp.int32)
    assigned = jnp.where(frame_pos < length, segment_row, -1)
    token_ids = jnp.arange(token_slots, dtype=jnp.int32)
    onehot = assigned[None, :] == token_ids[:, None]
    counts = jnp.sum(onehot.astype(jnp.float32), axis=1)
    return stacked, onehot.astype(jnp.bfloat16), jnp.maximum(counts, 1.0)


def encoder_part(stacked, onehot, counts, kernel, projector):
    hidden = jax.nn.gelu(jnp.dot(stacked, kernel, preferred_element_type=jnp.float32)).astype(
        jnp.bfloat16
    )
    summed = jnp.dot(onehot, hidden, preferred_element_type=jnp.float32)
    merged = (summed / counts[:, None]).astype(jnp.bfloat16)
    return jnp.dot(merged, projector, preferred_element_type=jnp.float32).astype(jnp.bfloat16)


def decoder_layer(token_rows, layer_gain, weight):
    values = token_rows.astype(jnp.float32)
    inverse_rms = lax.rsqrt(jnp.mean(values * values, axis=-1, keepdims=True) + 1e-06)
    normed = (values * inverse_rms * layer_gain).astype(jnp.bfloat16)
    return (values + jnp.dot(normed, weight, preferred_element_type=jnp.float32)).astype(
        jnp.bfloat16
    )


def per_device(frames, lengths, segments, section_weight, norm_gains):
    section_pos = lax.axis_index("section")
    sections = lax.axis_size("section")
    micro_count = frames.shape[0]
    tokens = frames.shape[1] // 4
    channels = frames.shape[2]
    model_width = section_weight.shape[2]

    section_slot = lax.all_gather(section_weight[0], "dp", axis=0, tiled=True)
    flattened = section_slot.reshape(-1)
    kernel = flattened[: 3 * channels * channels].reshape(3 * channels, channels)
    projector = flattened[
        3 * channels * channels : 3 * channels * channels + channels * model_width
    ].reshape(channels, model_width)
    layer_gain = norm_gains[jnp.maximum(section_pos - 1, 0)]
    stacked_all, onehot_all, counts_all = jax.vmap(
        lambda f, n, s: encoder_inputs(f, n, s, tokens)
    )(frames, lengths, segments)

    lag = 2
    route = [(i, i + 1) for i in range(sections - 1)]
    ticks = micro_count + lag * (sections - 1)
    zeros = jnp.zeros((tokens, model_width), jnp.bfloat16)

    def one_tick(tick, pending, received, stored, send=True, only=None):
        arrived = lax.ppermute(pending, "section", route) if send else received
        offset = tick - lag * section_pos
        active = (offset >= 0) & (offset < micro_count)
        micro_index = jnp.clip(offset, 0, micro_count - 1)

        def encode():
            return encoder_part(
                stacked_all[micro_index],
                onehot_all[micro_index],
                counts_all[micro_index],
                kernel,
                projector,
            )

        def decode():
            return decoder_layer(received, layer_gain, section_slot)

        def work():
            if only is not None:
                return encode() if only == "encode" else decode()
            return lax.cond(section_pos == 0, encode, decode)

        def keep():
            return lax.dynamic_slice_in_dim(stored, micro_index * tokens, tokens, 0)

        result = lax.cond(active, work, keep)
        stored = lax.dynamic_update_slice_in_dim(stored, result, micro_index * tokens, 0)
        return result, arrived, stored

    def tick_pair(pair, state):
        pending, received, stored = state
        pending, received, stored = one_tick(2 * pair + 1, pending, received, stored)
        return one_tick(2 * pair + 2, pending, received, stored)

    assert ticks % 2 == 0
    stored = jnp.zeros((micro_count * tokens, model_width), jnp.bfloat16)
    pending, _, stored = one_tick(0, zeros, zeros, stored, send=False, only="encode")
    pending, received, stored = lax.fori_loop(
        0, (ticks - 2) // 2, tick_pair, (pending, zeros, stored)
    )
    _, _, stored = one_tick(ticks - 1, pending, received, stored, send=False, only="decode")
    return stored.reshape(1, micro_count, tokens, model_width)


def solution(mesh):
    return jax.shard_map(
        per_device,
        mesh=mesh,
        in_specs=(P("dp", None, None), P("dp"), P("dp", None), P("section", "dp", None), P()),
        out_specs=P("section", "dp", None, None),
        check_vma=False,
    )
```

```python
import jax
import jax.numpy as jnp
from jax import lax
from jax.experimental import pallas as pl
from jax.sharding import PartitionSpec as P


def rows_matmul(left, weight, first_row, residual=None, column_block=512):
    rows, depth = left.shape
    width = weight.shape[1]

    def kernel(left_ref, weight_ref, *rest):
        out_ref = rest[-1]
        acc = jnp.dot(left_ref[...], weight_ref[...], preferred_element_type=jnp.float32)
        if residual is not None:
            acc = acc + rest[0][...].astype(jnp.float32)
        out_ref[...] = acc.astype(out_ref.dtype)

    in_specs = [
        pl.BlockSpec((rows, depth), lambda n: (0, 0)),
        pl.BlockSpec(
            (pl.Element(depth), pl.Element(column_block)),
            lambda n: (first_row, n * column_block),
        ),
    ]
    operands = [left, weight]
    if residual is not None:
        in_specs.append(pl.BlockSpec((rows, column_block), lambda n: (0, n)))
        operands.append(residual)
    return pl.pallas_call(
        kernel,
        grid=(width // column_block,),
        in_specs=in_specs,
        out_specs=pl.BlockSpec((rows, column_block), lambda n: (0, n)),
        out_shape=jax.ShapeDtypeStruct((rows, width), jnp.bfloat16),
    )(*operands)


def encoder_inputs(frame_block, length, segment_row, token_slots):
    half_frames = frame_block.shape[0] // 2
    channels = frame_block.shape[1]
    position = jnp.arange(frame_block.shape[0], dtype=jnp.int32)
    masked = jnp.where((position < 2 * length)[:, None], frame_block, jnp.zeros_like(frame_block))
    paired = masked.reshape(half_frames, 2 * channels)
    previous = jnp.concatenate(
        [jnp.zeros((1, channels), masked.dtype), paired[:-1, channels:]], axis=0
    )
    stacked = jnp.concatenate([previous, paired], axis=1)
    frame_pos = jnp.arange(half_frames, dtype=jnp.int32)
    assigned = jnp.where(frame_pos < length, segment_row, -1)
    token_ids = jnp.arange(token_slots, dtype=jnp.int32)
    onehot = assigned[None, :] == token_ids[:, None]
    counts = jnp.sum(onehot.astype(jnp.float32), axis=1)
    return stacked, onehot.astype(jnp.bfloat16), jnp.maximum(counts, 1.0)


def encoder_part(stacked, onehot, counts, kernel, slot, projector_row):
    hidden = jax.nn.gelu(jnp.dot(stacked, kernel, preferred_element_type=jnp.float32)).astype(
        jnp.bfloat16
    )
    summed = jnp.dot(onehot, hidden, preferred_element_type=jnp.float32)
    merged = (summed / counts[:, None]).astype(jnp.bfloat16)
    return rows_matmul(merged, slot, projector_row)


def decoder_layer(token_rows, layer_gain, weight):
    values = token_rows.astype(jnp.float32)
    inverse_rms = lax.rsqrt(jnp.mean(values * values, axis=-1, keepdims=True) + 1e-06)
    normed = (values * inverse_rms * layer_gain).astype(jnp.bfloat16)
    return (values + jnp.dot(normed, weight, preferred_element_type=jnp.float32)).astype(
        jnp.bfloat16
    )


def per_device(frames, lengths, segments, section_weight, norm_gains):
    section_pos = lax.axis_index("section")
    sections = lax.axis_size("section")
    micro_count = frames.shape[0]
    tokens = frames.shape[1] // 4
    channels = frames.shape[2]
    model_width = section_weight.shape[2]

    section_slot = lax.all_gather(section_weight[0], "dp", axis=0, tiled=True)
    kernel_rows = 3 * channels * channels // model_width
    kernel = section_slot[:kernel_rows].reshape(3 * channels, channels)
    layer_gain = norm_gains[jnp.maximum(section_pos - 1, 0)]
    stacked_all, onehot_all, counts_all = jax.vmap(
        lambda f, n, s: encoder_inputs(f, n, s, tokens)
    )(frames, lengths, segments)

    lag = 2
    route = [(i, i + 1) for i in range(sections - 1)]
    ticks = micro_count + lag * (sections - 1)
    zeros = jnp.zeros((tokens, model_width), jnp.bfloat16)

    def one_tick(tick, pending, received, stored, send=True, only=None):
        arrived = lax.ppermute(pending, "section", route) if send else received
        offset = tick - lag * section_pos
        active = (offset >= 0) & (offset < micro_count)
        micro_index = jnp.clip(offset, 0, micro_count - 1)

        def encode():
            return encoder_part(
                stacked_all[micro_index],
                onehot_all[micro_index],
                counts_all[micro_index],
                kernel,
                section_slot,
                kernel_rows,
            )

        def decode():
            return decoder_layer(received, layer_gain, section_slot)

        def work():
            if only is not None:
                return encode() if only == "encode" else decode()
            return lax.cond(section_pos == 0, encode, decode)

        def keep():
            return lax.dynamic_slice_in_dim(stored, micro_index * tokens, tokens, 0)

        result = lax.cond(active, work, keep)
        stored = lax.dynamic_update_slice_in_dim(stored, result, micro_index * tokens, 0)
        return result, arrived, stored

    def tick_pair(pair, state):
        pending, received, stored = state
        pending, received, stored = one_tick(2 * pair + 1, pending, received, stored)
        return one_tick(2 * pair + 2, pending, received, stored)

    assert ticks % 2 == 0
    stored = jnp.zeros((micro_count * tokens, model_width), jnp.bfloat16)
    pending, _, stored = one_tick(0, zeros, zeros, stored, send=False, only="encode")
    pending, received, stored = lax.fori_loop(
        0, (ticks - 2) // 2, tick_pair, (pending, zeros, stored)
    )
    _, _, stored = one_tick(ticks - 1, pending, received, stored, send=False, only="decode")
    return stored.reshape(1, micro_count, tokens, model_width)


def solution(mesh):
    return jax.shard_map(
        per_device,
        mesh=mesh,
        in_specs=(P("dp", None, None), P("dp"), P("dp", None), P("section", "dp", None), P()),
        out_specs=P("section", "dp", None, None),
        check_vma=False,
    )
```

```python
import jax
import jax.numpy as jnp
from jax import lax
from jax.experimental import pallas as pl
from jax.experimental.pallas import tpu as pltpu
from jax.sharding import PartitionSpec as P


def kernel_relayout(slot, rows, width):
    depth = slot.shape[1]
    lane = 128
    per = depth * 5 // width
    group_in, group_out = 5 * 16, per * 16

    def body(in_ref, out_ref, wide_in, wide_out):
        for t in range(depth // lane):
            wide_in[:, t, :] = in_ref[:, pl.ds(t * lane, lane)].astype(jnp.float32)
        for s in range(per):
            for t in range(width // lane):
                a, b = divmod(s * width + t * lane, depth)
                wide_out[pl.ds(s, 16, stride=per), t, :] = wide_in[
                    pl.ds(a, 16, stride=5), b // lane, :
                ]
        for t in range(width // lane):
            out_ref[:, pl.ds(t * lane, lane)] = wide_out[:, t, :].astype(out_ref.dtype)

    return pl.pallas_call(
        body,
        grid=(rows // group_in,),
        in_specs=[pl.BlockSpec((group_in, depth), lambda q: (q, 0))],
        out_specs=pl.BlockSpec((group_out, width), lambda q: (q, 0)),
        out_shape=jax.ShapeDtypeStruct((rows * depth // width, width), slot.dtype),
        scratch_shapes=[
            pltpu.VMEM((group_in, depth // lane, lane), jnp.float32),
            pltpu.VMEM((group_out, width // lane, lane), jnp.float32),
        ],
    )(slot)


def rows_matmul(left, weight, first_row, residual=None, column_block=512):
    rows, depth = left.shape
    width = weight.shape[1]

    def kernel(left_ref, weight_ref, *rest):
        out_ref = rest[-1]
        acc = jnp.dot(left_ref[...], weight_ref[...], preferred_element_type=jnp.float32)
        if residual is not None:
            acc = acc + rest[0][...].astype(jnp.float32)
        out_ref[...] = acc.astype(out_ref.dtype)

    in_specs = [
        pl.BlockSpec((rows, depth), lambda n: (0, 0)),
        pl.BlockSpec(
            (pl.Element(depth), pl.Element(column_block)),
            lambda n: (first_row, n * column_block),
        ),
    ]
    operands = [left, weight]
    if residual is not None:
        in_specs.append(pl.BlockSpec((rows, column_block), lambda n: (0, n)))
        operands.append(residual)
    return pl.pallas_call(
        kernel,
        grid=(width // column_block,),
        in_specs=in_specs,
        out_specs=pl.BlockSpec((rows, column_block), lambda n: (0, n)),
        out_shape=jax.ShapeDtypeStruct((rows, width), jnp.bfloat16),
    )(*operands)


def encoder_inputs(frame_block, length, segment_row, token_slots):
    half_frames = frame_block.shape[0] // 2
    channels = frame_block.shape[1]
    position = jnp.arange(frame_block.shape[0], dtype=jnp.int32)
    masked = jnp.where((position < 2 * length)[:, None], frame_block, jnp.zeros_like(frame_block))
    paired = masked.reshape(half_frames, 2 * channels)
    previous = jnp.concatenate(
        [jnp.zeros((1, channels), masked.dtype), paired[:-1, channels:]], axis=0
    )
    stacked = jnp.concatenate([previous, paired], axis=1)
    frame_pos = jnp.arange(half_frames, dtype=jnp.int32)
    assigned = jnp.where(frame_pos < length, segment_row, -1)
    token_ids = jnp.arange(token_slots, dtype=jnp.int32)
    onehot = assigned[None, :] == token_ids[:, None]
    counts = jnp.sum(onehot.astype(jnp.float32), axis=1)
    return stacked, onehot.astype(jnp.bfloat16), jnp.maximum(counts, 1.0)


def encoder_part(stacked, onehot, counts, kernel, slot, projector_row):
    hidden = jax.nn.gelu(jnp.dot(stacked, kernel, preferred_element_type=jnp.float32)).astype(
        jnp.bfloat16
    )
    summed = jnp.dot(onehot, hidden, preferred_element_type=jnp.float32)
    merged = (summed / counts[:, None]).astype(jnp.bfloat16)
    return rows_matmul(merged, slot, projector_row)


def decoder_layer(token_rows, layer_gain, weight):
    values = token_rows.astype(jnp.float32)
    inverse_rms = lax.rsqrt(jnp.mean(values * values, axis=-1, keepdims=True) + 1e-06)
    normed = (values * inverse_rms * layer_gain).astype(jnp.bfloat16)
    return (values + jnp.dot(normed, weight, preferred_element_type=jnp.float32)).astype(
        jnp.bfloat16
    )


def per_device(frames, lengths, segments, section_weight, norm_gains):
    section_pos = lax.axis_index("section")
    sections = lax.axis_size("section")
    micro_count = frames.shape[0]
    tokens = frames.shape[1] // 4
    channels = frames.shape[2]
    model_width = section_weight.shape[2]

    section_slot = lax.all_gather(section_weight[0], "dp", axis=0, tiled=True)
    kernel_rows = 3 * channels * channels // model_width
    kernel = kernel_relayout(section_slot, kernel_rows, channels)
    layer_gain = norm_gains[jnp.maximum(section_pos - 1, 0)]
    stacked_all, onehot_all, counts_all = jax.vmap(
        lambda f, n, s: encoder_inputs(f, n, s, tokens)
    )(frames, lengths, segments)

    lag = 2
    route = [(i, i + 1) for i in range(sections - 1)]
    ticks = micro_count + lag * (sections - 1)
    zeros = jnp.zeros((tokens, model_width), jnp.bfloat16)

    def one_tick(tick, pending, received, stored, send=True, only=None):
        arrived = lax.ppermute(pending, "section", route) if send else received
        offset = tick - lag * section_pos
        active = (offset >= 0) & (offset < micro_count)
        micro_index = jnp.clip(offset, 0, micro_count - 1)

        def encode():
            return encoder_part(
                stacked_all[micro_index],
                onehot_all[micro_index],
                counts_all[micro_index],
                kernel,
                section_slot,
                kernel_rows,
            )

        def decode():
            return decoder_layer(received, layer_gain, section_slot)

        def work():
            if only is not None:
                return encode() if only == "encode" else decode()
            return lax.cond(section_pos == 0, encode, decode)

        def keep():
            return lax.dynamic_slice_in_dim(stored, micro_index * tokens, tokens, 0)

        result = lax.cond(active, work, keep)
        stored = lax.dynamic_update_slice_in_dim(stored, result, micro_index * tokens, 0)
        return result, arrived, stored

    def tick_pair(pair, state):
        pending, received, stored = state
        pending, received, stored = one_tick(2 * pair + 1, pending, received, stored)
        return one_tick(2 * pair + 2, pending, received, stored)

    assert ticks % 2 == 0
    stored = jnp.zeros((micro_count * tokens, model_width), jnp.bfloat16)
    pending, _, stored = one_tick(0, zeros, zeros, stored, send=False, only="encode")
    pending, received, stored = lax.fori_loop(
        0, (ticks - 2) // 2, tick_pair, (pending, zeros, stored)
    )
    _, _, stored = one_tick(ticks - 1, pending, received, stored, send=False, only="decode")
    return stored.reshape(1, micro_count, tokens, model_width)


def solution(mesh):
    return jax.shard_map(
        per_device,
        mesh=mesh,
        in_specs=(P("dp", None, None), P("dp"), P("dp", None), P("section", "dp", None), P()),
        out_specs=P("section", "dp", None, None),
        check_vma=False,
    )
```

```python
import jax
import jax.numpy as jnp
from jax import lax
from jax.experimental import pallas as pl
from jax.sharding import PartitionSpec as P


def rows_matmul(left, weight, first_row, residual=None, column_block=512):
    rows, depth = left.shape
    width = weight.shape[1]

    def kernel(left_ref, weight_ref, *rest):
        out_ref = rest[-1]
        acc = jnp.dot(left_ref[...], weight_ref[...], preferred_element_type=jnp.float32)
        if residual is not None:
            acc = acc + rest[0][...].astype(jnp.float32)
        out_ref[...] = acc.astype(out_ref.dtype)

    in_specs = [
        pl.BlockSpec((rows, depth), lambda n: (0, 0)),
        pl.BlockSpec(
            (pl.Element(depth), pl.Element(column_block)),
            lambda n: (first_row, n * column_block),
        ),
    ]
    operands = [left, weight]
    if residual is not None:
        in_specs.append(pl.BlockSpec((rows, column_block), lambda n: (0, n)))
        operands.append(residual)
    return pl.pallas_call(
        kernel,
        grid=(width // column_block,),
        in_specs=in_specs,
        out_specs=pl.BlockSpec((rows, column_block), lambda n: (0, n)),
        out_shape=jax.ShapeDtypeStruct((rows, width), jnp.bfloat16),
    )(*operands)


def encoder_inputs(frame_block, length, segment_row, token_slots):
    half_frames = frame_block.shape[0] // 2
    channels = frame_block.shape[1]
    position = jnp.arange(frame_block.shape[0], dtype=jnp.int32)
    masked = jnp.where((position < 2 * length)[:, None], frame_block, jnp.zeros_like(frame_block))
    paired = masked.reshape(half_frames, 2 * channels)
    previous = jnp.concatenate(
        [jnp.zeros((1, channels), masked.dtype), paired[:-1, channels:]], axis=0
    )
    stacked = jnp.concatenate([previous, paired], axis=1)
    frame_pos = jnp.arange(half_frames, dtype=jnp.int32)
    assigned = jnp.where(frame_pos < length, segment_row, -1)
    token_ids = jnp.arange(token_slots, dtype=jnp.int32)
    onehot = assigned[None, :] == token_ids[:, None]
    counts = jnp.sum(onehot.astype(jnp.float32), axis=1)
    return stacked, onehot.astype(jnp.bfloat16), jnp.maximum(counts, 1.0)


def encoder_part(stacked, onehot, counts, kernel, slot, projector_row):
    hidden = jax.nn.gelu(jnp.dot(stacked, kernel, preferred_element_type=jnp.float32)).astype(
        jnp.bfloat16
    )
    summed = jnp.dot(onehot, hidden, preferred_element_type=jnp.float32)
    merged = (summed / counts[:, None]).astype(jnp.bfloat16)
    return rows_matmul(merged, slot, projector_row, column_block=1024)


def decoder_layer(token_rows, layer_gain, weight):
    values = token_rows.astype(jnp.float32)
    inverse_rms = lax.rsqrt(jnp.mean(values * values, axis=-1, keepdims=True) + 1e-06)
    normed = (values * inverse_rms * layer_gain).astype(jnp.bfloat16)
    return (values + jnp.dot(normed, weight, preferred_element_type=jnp.float32)).astype(
        jnp.bfloat16
    )


def per_device(frames, lengths, segments, section_weight, norm_gains):
    section_pos = lax.axis_index("section")
    sections = lax.axis_size("section")
    micro_count = frames.shape[0]
    tokens = frames.shape[1] // 4
    channels = frames.shape[2]
    model_width = section_weight.shape[2]

    section_slot = lax.all_gather(section_weight[0], "dp", axis=0, tiled=True)
    kernel_rows = 3 * channels * channels // model_width
    kernel = section_slot[:kernel_rows].reshape(3 * channels, channels)
    layer_gain = norm_gains[jnp.maximum(section_pos - 1, 0)]
    stacked_all, onehot_all, counts_all = jax.vmap(
        lambda f, n, s: encoder_inputs(f, n, s, tokens)
    )(frames, lengths, segments)

    lag = 2
    route = [(i, i + 1) for i in range(sections - 1)]
    ticks = micro_count + lag * (sections - 1)
    zeros = jnp.zeros((tokens, model_width), jnp.bfloat16)

    def one_tick(tick, pending, received, stored, send=True, only=None):
        arrived = lax.ppermute(pending, "section", route) if send else received
        offset = tick - lag * section_pos
        active = (offset >= 0) & (offset < micro_count)
        micro_index = jnp.clip(offset, 0, micro_count - 1)

        def encode():
            return encoder_part(
                stacked_all[micro_index],
                onehot_all[micro_index],
                counts_all[micro_index],
                kernel,
                section_slot,
                kernel_rows,
            )

        def decode():
            return decoder_layer(received, layer_gain, section_slot)

        def work():
            if only is not None:
                return encode() if only == "encode" else decode()
            return lax.cond(section_pos == 0, encode, decode)

        def keep():
            return lax.dynamic_slice_in_dim(stored, micro_index * tokens, tokens, 0)

        result = lax.cond(active, work, keep)
        stored = lax.dynamic_update_slice_in_dim(stored, result, micro_index * tokens, 0)
        return result, arrived, stored

    def tick_pair(pair, state):
        pending, received, stored = state
        pending, received, stored = one_tick(2 * pair + 1, pending, received, stored)
        return one_tick(2 * pair + 2, pending, received, stored)

    assert ticks % 2 == 0
    stored = jnp.zeros((micro_count * tokens, model_width), jnp.bfloat16)
    pending, _, stored = one_tick(0, zeros, zeros, stored, send=False, only="encode")
    pending, received, stored = lax.fori_loop(
        0, (ticks - 2) // 2, tick_pair, (pending, zeros, stored)
    )
    _, _, stored = one_tick(ticks - 1, pending, received, stored, send=False, only="decode")
    return stored.reshape(1, micro_count, tokens, model_width)


def solution(mesh):
    return jax.shard_map(
        per_device,
        mesh=mesh,
        in_specs=(P("dp", None, None), P("dp"), P("dp", None), P("section", "dp", None), P()),
        out_specs=P("section", "dp", None, None),
        check_vma=False,
    )
```

```python
import jax
import jax.numpy as jnp
from jax import lax
from jax.experimental import pallas as pl
from jax.sharding import PartitionSpec as P


def rows_matmul(left, weight, first_row, residual=None, column_block=512):
    rows, depth = left.shape
    width = weight.shape[1]

    def kernel(left_ref, weight_ref, *rest):
        out_ref = rest[-1]
        acc = jnp.dot(left_ref[...], weight_ref[...], preferred_element_type=jnp.float32)
        if residual is not None:
            acc = acc + rest[0][...].astype(jnp.float32)
        out_ref[...] = acc.astype(out_ref.dtype)

    in_specs = [
        pl.BlockSpec((rows, depth), lambda n: (0, 0)),
        pl.BlockSpec(
            (pl.Element(depth), pl.Element(column_block)),
            lambda n: (first_row, n * column_block),
        ),
    ]
    operands = [left, weight]
    if residual is not None:
        in_specs.append(pl.BlockSpec((rows, column_block), lambda n: (0, n)))
        operands.append(residual)
    return pl.pallas_call(
        kernel,
        grid=(width // column_block,),
        in_specs=in_specs,
        out_specs=pl.BlockSpec((rows, column_block), lambda n: (0, n)),
        out_shape=jax.ShapeDtypeStruct((rows, width), jnp.bfloat16),
    )(*operands)


def encoder_inputs(frame_block, length, segment_row, token_slots):
    half_frames = frame_block.shape[0] // 2
    channels = frame_block.shape[1]
    position = jnp.arange(frame_block.shape[0], dtype=jnp.int32)
    masked = jnp.where((position < 2 * length)[:, None], frame_block, jnp.zeros_like(frame_block))
    paired = masked.reshape(half_frames, 2 * channels)
    previous = jnp.concatenate(
        [jnp.zeros((1, channels), masked.dtype), paired[:-1, channels:]], axis=0
    )
    stacked = jnp.concatenate([previous, paired], axis=1)
    frame_pos = jnp.arange(half_frames, dtype=jnp.int32)
    assigned = jnp.where(frame_pos < length, segment_row, -1)
    token_ids = jnp.arange(token_slots, dtype=jnp.int32)
    onehot = assigned[None, :] == token_ids[:, None]
    counts = jnp.sum(onehot.astype(jnp.float32), axis=1)
    return stacked, onehot.astype(jnp.bfloat16), jnp.maximum(counts, 1.0)


def encoder_part(stacked, onehot, counts, kernel, slot, projector_row):
    hidden = jax.nn.gelu(jnp.dot(stacked, kernel, preferred_element_type=jnp.float32)).astype(
        jnp.bfloat16
    )
    summed = jnp.dot(onehot, hidden, preferred_element_type=jnp.float32)
    merged = (summed / counts[:, None]).astype(jnp.bfloat16)
    return rows_matmul(merged, slot, projector_row, column_block=2048)


def decoder_layer(token_rows, layer_gain, weight):
    values = token_rows.astype(jnp.float32)
    inverse_rms = lax.rsqrt(jnp.mean(values * values, axis=-1, keepdims=True) + 1e-06)
    normed = (values * inverse_rms * layer_gain).astype(jnp.bfloat16)
    return (values + jnp.dot(normed, weight, preferred_element_type=jnp.float32)).astype(
        jnp.bfloat16
    )


def per_device(frames, lengths, segments, section_weight, norm_gains):
    section_pos = lax.axis_index("section")
    sections = lax.axis_size("section")
    micro_count = frames.shape[0]
    tokens = frames.shape[1] // 4
    channels = frames.shape[2]
    model_width = section_weight.shape[2]

    section_slot = lax.all_gather(section_weight[0], "dp", axis=0, tiled=True)
    kernel_rows = 3 * channels * channels // model_width
    kernel = section_slot[:kernel_rows].reshape(3 * channels, channels)
    layer_gain = norm_gains[jnp.maximum(section_pos - 1, 0)]
    stacked_all, onehot_all, counts_all = jax.vmap(
        lambda f, n, s: encoder_inputs(f, n, s, tokens)
    )(frames, lengths, segments)

    lag = 2
    route = [(i, i + 1) for i in range(sections - 1)]
    ticks = micro_count + lag * (sections - 1)
    zeros = jnp.zeros((tokens, model_width), jnp.bfloat16)

    def one_tick(tick, pending, received, stored, send=True, only=None):
        arrived = lax.ppermute(pending, "section", route) if send else received
        offset = tick - lag * section_pos
        active = (offset >= 0) & (offset < micro_count)
        micro_index = jnp.clip(offset, 0, micro_count - 1)

        def encode():
            return encoder_part(
                stacked_all[micro_index],
                onehot_all[micro_index],
                counts_all[micro_index],
                kernel,
                section_slot,
                kernel_rows,
            )

        def decode():
            return decoder_layer(received, layer_gain, section_slot)

        def work():
            if only is not None:
                return encode() if only == "encode" else decode()
            return lax.cond(section_pos == 0, encode, decode)

        def keep():
            return lax.dynamic_slice_in_dim(stored, micro_index * tokens, tokens, 0)

        result = lax.cond(active, work, keep)
        stored = lax.dynamic_update_slice_in_dim(stored, result, micro_index * tokens, 0)
        return result, arrived, stored

    def tick_pair(pair, state):
        pending, received, stored = state
        pending, received, stored = one_tick(2 * pair + 1, pending, received, stored)
        return one_tick(2 * pair + 2, pending, received, stored)

    assert ticks % 2 == 0
    stored = jnp.zeros((micro_count * tokens, model_width), jnp.bfloat16)
    pending, _, stored = one_tick(0, zeros, zeros, stored, send=False, only="encode")
    pending, received, stored = lax.fori_loop(
        0, (ticks - 2) // 2, tick_pair, (pending, zeros, stored)
    )
    _, _, stored = one_tick(ticks - 1, pending, received, stored, send=False, only="decode")
    return stored.reshape(1, micro_count, tokens, model_width)


def solution(mesh):
    return jax.shard_map(
        per_device,
        mesh=mesh,
        in_specs=(P("dp", None, None), P("dp"), P("dp", None), P("section", "dp", None), P()),
        out_specs=P("section", "dp", None, None),
        check_vma=False,
    )
```
